128 devices in a mesh: chan: 16 (over y_lo, z, core), band: 8 (over x, y_hi).
Axes of the slice: x: 4, y: 4 (y_hi: 2, y_lo: 2; y = y_hi * 2 + y_lo), z: 4, core: 2. Of those that a mesh axis runs over, the one named last changes fastest.
Arguments:
- raw: bfloat16 [128, 2560, 2747], P(('chan', 'band')), may hold values from -600 to 600
- offsets: int32 [128], P(('chan', 'band')), may hold values from 0 to 127
- taps: bfloat16 [63], replicated, may hold values from -0.75 to 0.75
- partner: int32 [2, 16], replicated, may hold values from 0 to 15, as said below
Outputs:
- cross: float32 [2, 2, 128, 2560, 160], P(None, None, 'band', 'chan')
The draws below stay inside these ranges and needn't reach their ends.
Inputs may be any that keep to these rules, and one draw needn't show every extreme that they name: For each round r there is one number M of 1 to 15 with partner[r, a] = a xor M for every block a; the two rounds' numbers differ.
All inputs are finite; a program needn't handle non-finite values.
Results may differ from the reference program's by a relative error of at most 0.0041.
Values may be sent and summed in bfloat16 or wider, within the bound.
No kernel may reach another device: no remote copies, remote signals or barrier semaphores. Data moves between devices by JAX's collectives and lax.ppermute only.
A program may use at most 128 MiB of HBM per device.

```python
import math
import jax
import jax.numpy as jnp
from jax import lax

CH = 2560
DEC = 10
TAPS = 63
W = 256
NF = 128
HALF = 32
SLACK = 127
ROUNDS = 2
WINDOWS = 128
BLOCKS = 16
CB = 160
SEG = 2747


def draw_raw(key, part):
    first_key, second_key, third_key = jax.random.split(key, 3)
    base = jnp.clip(jax.random.normal(first_key, (WINDOWS, CH, SEG), jnp.float32), -6.0, 6.0)
    chan_scale = 10.0 ** jax.random.uniform(second_key, (1, CH, 1), jnp.float32)
    block_count = SEG // 160 + 1
    time_scale = 10.0 ** jax.random.uniform(third_key, (WINDOWS, 1, block_count), jnp.float32)
    time_scale = jnp.repeat(time_scale, 160, axis=2)[:, :, :SEG]
    return (base * chan_scale * time_scale).astype(jnp.bfloat16)


def draw_offsets(key, part):
    first_key, second_key = jax.random.split(key, 2)
    values = jax.random.randint(first_key, (WINDOWS,), 0, SLACK + 1, jnp.int32)
    where_top = jax.random.randint(second_key, (), 0, WINDOWS, jnp.int32)
    values = values.at[where_top].set(SLACK)
    values = values.at[(where_top + 1) % WINDOWS].set(0)
    return values.astype(jnp.int32)


def draw_partner(key, part):
    first_key, second_key = jax.random.split(jax.random.fold_in(key, 7), 2)
    first_number = jax.random.randint(first_key, (), 1, BLOCKS, jnp.int32)
    second_number = jax.random.randint(second_key, (), 1, BLOCKS - 1, jnp.int32)
    second_number = jnp.where(second_number >= first_number, second_number + 1, second_number)
    numbers = jnp.stack([first_number, second_number]).astype(jnp.int32)
    blocks = jnp.arange(BLOCKS, dtype=jnp.int32)[None, :]
    return jnp.bitwise_xor(blocks, numbers[:, None]).astype(jnp.int32)


def normal_values(key, extent, width, limit, kind=jnp.bfloat16):
    array = jax.random.normal(key, extent, jnp.float32) * width
    return jnp.minimum(jnp.maximum(array, -limit), limit).astype(kind)


def setup_inputs(seed: int = 0) -> dict:
    seeds = jax.random.split(jax.random.key(seed), 5)
    return {
        "raw": draw_raw(jax.random.fold_in(seeds[4], 71), 0),
        "offsets": draw_offsets(jax.random.fold_in(seeds[4], 71), 0),
        "taps": normal_values(seeds[2], (TAPS,), TAPS ** -0.5, 0.75),
        "partner": draw_partner(jax.random.fold_in(seeds[4], 71), 0),
    }


def mean_matrix(length, half):
    rows = jnp.arange(length, dtype=jnp.int32)[:, None]
    cols = jnp.arange(length, dtype=jnp.int32)[None, :]
    begins = jnp.clip(cols - half, 0, length - 2 * half - 1)
    inside = (rows >= begins) & (rows <= begins + 2 * half)
    return inside.astype(jnp.float32)

def dft_table(length, bins):
    samples = jnp.arange(length, dtype=jnp.int32)[:, None]
    freqs = jnp.arange(bins, dtype=jnp.int32)[None, :]
    phase = samples * freqs % length
    angle = phase.astype(jnp.float32) * (2.0 * math.pi / length)
    return jnp.concatenate([jnp.cos(angle), -jnp.sin(angle)], axis=1)

def window_spectrum(segment, offset, taps):
    span = DEC * (W - 1) + TAPS
    piece = lax.dynamic_slice_in_dim(segment, offset.astype(jnp.int32), span, 1).astype(jnp.float32)
    decimated = jnp.zeros((CH, W), jnp.float32)
    for tap_index in range(TAPS):
        decimated = decimated + taps[tap_index].astype(jnp.float32) * piece[:, tap_index:tap_index + DEC * (W - 1) + 1:DEC]
    level = jnp.dot(jnp.abs(decimated), mean_matrix(W, HALF), precision=lax.Precision.HIGHEST) / (2 * HALF + 1)
    normed = decimated / (level + 1e-05)
    spectrum = lax.dot_general(dft_table(W, NF), normed, (((0,), (1,)), ((), ())), precision=lax.Precision.HIGHEST)
    return spectrum.reshape(2, NF, CH).astype(jnp.bfloat16)

def reference(raw, offsets, taps, partner):
    spectra = lax.map(lambda pair: window_spectrum(pair[0], pair[1], taps), (raw, offsets))
    blocks = spectra.reshape(WINDOWS, 2, NF, BLOCKS, CB)
    factor = 1.0 / (W * math.sqrt(WINDOWS))
    results = []
    for round_index in range(ROUNDS):

        def one_block(block_index):
            own_block = lax.dynamic_index_in_dim(blocks, block_index, 3, keepdims=False).astype(jnp.float32)
            other_index = partner[round_index, block_index].astype(jnp.int32)
            other_block = lax.dynamic_index_in_dim(blocks, other_index, 3, keepdims=False).astype(jnp.float32)
            product = jnp.einsum('wpfi,wqfj->pqfij', own_block, other_block, precision=lax.Precision.HIGHEST)
            real_part = product[0, 0] + product[1, 1]
            imag_part = product[1, 0] - product[0, 1]
            return jnp.stack([real_part, imag_part]) * factor
        per_block = lax.map(one_block, jnp.arange(BLOCKS, dtype=jnp.int32))
        results.append(per_block.transpose(1, 2, 0, 3, 4).reshape(2, NF, CH, CB))
    return jnp.stack(results)
```

```python
import math

import jax
import jax.numpy as jnp
from jax import lax
from jax.sharding import PartitionSpec as P

DEC = 10
TAPS = 63
W = 256
NF = 128
HALF = 32


def mean_matrix(length, half):
    rows = jnp.arange(length, dtype=jnp.int32)[:, None]
    cols = jnp.arange(length, dtype=jnp.int32)[None, :]
    begins = jnp.clip(cols - half, 0, length - 2 * half - 1)
    inside = (rows >= begins) & (rows <= begins + 2 * half)
    return inside.astype(jnp.float32)


def dft_table(length, bins):
    samples = jnp.arange(length, dtype=jnp.int32)[:, None]
    freqs = jnp.arange(bins, dtype=jnp.int32)[None, :]
    phase = samples * freqs % length
    angle = phase.astype(jnp.float32) * (2.0 * math.pi / length)
    return jnp.concatenate([jnp.cos(angle), -jnp.sin(angle)], axis=1)


def filter_table(taps, phases):
    padded = jnp.pad(taps, (0, phases * DEC - TAPS))
    grid = padded.reshape(phases, DEC)
    rows = jnp.arange(W + phases - 1, dtype=jnp.int32)[:, None]
    cols = jnp.arange(W, dtype=jnp.int32)[None, :]
    onehot = (
        (rows - cols)[None, :, :] == jnp.arange(phases, dtype=jnp.int32)[:, None, None]
    ).astype(jnp.bfloat16)
    table = jnp.einsum("jqn,jr->qrn", onehot, grid, preferred_element_type=jnp.float32)
    return table.reshape((W + phases - 1) * DEC, W).astype(jnp.bfloat16)


def window_spectrum(segment, offset, table, level_matrix, transform):
    span = table.shape[0]
    piece = lax.dynamic_slice_in_dim(segment, offset, span, 1)
    decimated = jnp.dot(piece, table, preferred_element_type=jnp.float32)
    level = jnp.dot(jnp.abs(decimated), level_matrix, precision=lax.Precision.HIGHEST) / (
        2 * HALF + 1
    )
    normed = decimated / (level + 1e-05)
    spectrum = lax.dot_general(
        transform, normed, (((0,), (1,)), ((), ())), precision=lax.Precision.HIGHEST
    )
    return spectrum.reshape(2, NF, segment.shape[0]).astype(jnp.bfloat16)


def body(raw, offsets, taps, partner):
    phases = (TAPS + DEC - 1) // DEC
    table = filter_table(taps, phases)
    level_matrix = mean_matrix(W, HALF)
    transform = dft_table(W, NF)
    spectra = jnp.stack([window_spectrum(raw[0], offsets[0], table, level_matrix, transform)])
    chan_count = lax.axis_size("chan")
    band_count = lax.axis_size("band")
    window_count, part_count, bin_count, channel_count = spectra.shape
    arranged = spectra.reshape(
        window_count,
        part_count,
        band_count,
        bin_count // band_count,
        chan_count,
        channel_count // chan_count,
    )
    arranged = arranged.transpose(4, 2, 0, 1, 3, 5).reshape(
        chan_count * band_count * window_count,
        part_count,
        bin_count // band_count,
        channel_count // chan_count,
    )
    local = lax.all_to_all(arranged, ("chan", "band"), split_axis=0, concat_axis=0, tiled=True)
    width = local.shape[3]
    chan_count_static = chan_count

    def exchange(rows, number):
        def branch(shift):
            pairs = [(a, a ^ shift) for a in range(chan_count_static)]
            return lambda x: lax.ppermute(x, "chan", pairs)

        branches = [branch(shift) for shift in range(1, chan_count_static)]
        return lax.switch(number - 1, branches, rows)

    first_other = exchange(local, partner[0, 0])
    second_other = exchange(local, partner[1, 0])
    factor = 1.0 / (W * math.sqrt(local.shape[0]))

    def stack_pair(other_rows):
        product = jnp.einsum(
            "wpfi,wqfj->fpqij", local, other_rows, preferred_element_type=jnp.float32
        )
        real_part = product[:, 0, 0] + product[:, 1, 1]
        imag_part = product[:, 1, 0] - product[:, 0, 1]
        return jnp.stack([real_part, imag_part]) * factor

    return jnp.stack([stack_pair(first_other), stack_pair(second_other)])


def solution(mesh):
    return jax.shard_map(
        body,
        mesh=mesh,
        in_specs=(P(("chan", "band"), None, None), P(("chan", "band")), P(), P()),
        out_specs=P(None, None, "band", "chan", None),
        check_vma=False,
    )
```

```python
import math

import jax
import jax.numpy as jnp
from jax import lax
from jax.sharding import PartitionSpec as P

DEC = 10
TAPS = 63
W = 256
NF = 128
HALF = 32


def mean_matrix(length, half):
    rows = jnp.arange(length, dtype=jnp.int32)[:, None]
    cols = jnp.arange(length, dtype=jnp.int32)[None, :]
    begins = jnp.clip(cols - half, 0, length - 2 * half - 1)
    inside = (rows >= begins) & (rows <= begins + 2 * half)
    return inside.astype(jnp.float32)


def dft_table(length, bins):
    samples = jnp.arange(length, dtype=jnp.int32)[:, None]
    freqs = jnp.arange(bins, dtype=jnp.int32)[None, :]
    phase = samples * freqs % length
    angle = phase.astype(jnp.float32) * (2.0 * math.pi / length)
    return jnp.concatenate([jnp.cos(angle), -jnp.sin(angle)], axis=1)


def filter_table(taps, phases):
    padded = jnp.pad(taps, (0, phases * DEC - TAPS))
    grid = padded.reshape(phases, DEC)
    rows = jnp.arange(W + phases - 1, dtype=jnp.int32)[:, None]
    cols = jnp.arange(W, dtype=jnp.int32)[None, :]
    onehot = (
        (rows - cols)[None, :, :] == jnp.arange(phases, dtype=jnp.int32)[:, None, None]
    ).astype(jnp.bfloat16)
    table = jnp.einsum("jqn,jr->qrn", onehot, grid, preferred_element_type=jnp.float32)
    return table.reshape((W + phases - 1) * DEC, W).astype(jnp.bfloat16)


def window_spectrum(segment, offset, table, level_matrix, transform):
    span = table.shape[0]
    piece = lax.dynamic_slice_in_dim(segment, offset, span, 1)
    decimated = jnp.dot(piece, table, preferred_element_type=jnp.float32)
    level = jnp.dot(jnp.abs(decimated), level_matrix, precision=lax.Precision.HIGHEST) / (
        2 * HALF + 1
    )
    normed = decimated / (level + 1e-05)
    spectrum = lax.dot_general(
        transform, normed, (((0,), (1,)), ((), ())), precision=lax.Precision.HIGHEST
    )
    return spectrum.reshape(2, NF, segment.shape[0]).astype(jnp.bfloat16)


def body(raw, offsets, taps, partner):
    phases = (TAPS + DEC - 1) // DEC
    table = filter_table(taps, phases)
    level_matrix = mean_matrix(W, HALF)
    transform = dft_table(W, NF)
    spectra = jnp.stack([window_spectrum(raw[0], offsets[0], table, level_matrix, transform)])
    chan_count = lax.axis_size("chan")
    band_count = lax.axis_size("band")
    window_count, part_count, bin_count, channel_count = spectra.shape
    arranged = spectra.reshape(
        window_count,
        part_count,
        band_count,
        bin_count // band_count,
        chan_count,
        channel_count // chan_count,
    )
    arranged = arranged.transpose(4, 2, 0, 1, 3, 5).reshape(
        chan_count * band_count * window_count,
        part_count,
        bin_count // band_count,
        channel_count // chan_count,
    )
    local = lax.all_to_all(arranged, ("chan", "band"), split_axis=0, concat_axis=0, tiled=True)
    width = local.shape[3]
    chan_count_static = chan_count

    def exchange(rows, number):
        def branch(shift):
            pairs = [(a, a ^ shift) for a in range(chan_count_static)]
            return lambda x: lax.ppermute(x, "chan", pairs)

        branches = [branch(shift) for shift in range(1, chan_count_static)]
        return lax.switch(number - 1, branches, rows)

    first_other = exchange(local, partner[0, 0])
    second_other = exchange(local, partner[1, 0])
    factor = 1.0 / (W * math.sqrt(local.shape[0]))
    windows, parts, bins, width = local.shape
    columns = []
    for other_rows in (first_other, second_other):
        real_rows = other_rows[:, 0]
        imag_rows = other_rows[:, 1]
        columns.append(other_rows)
        columns.append(jnp.stack([-imag_rows, real_rows], axis=1))
    mixed = jnp.stack(columns, axis=3).reshape(windows * parts, bins, len(columns), width)
    own = local.reshape(windows * parts, bins, width)
    own = jnp.broadcast_to(own[None], (len(columns),) + own.shape)
    mixed = jnp.moveaxis(mixed, 2, 0)
    product = jnp.einsum("qkfi,qkfj->qfij", own, mixed, preferred_element_type=jnp.float32)
    return (product * factor).reshape(2, 2, bins, width, width)


def solution(mesh):
    return jax.shard_map(
        body,
        mesh=mesh,
        in_specs=(P(("chan", "band"), None, None), P(("chan", "band")), P(), P()),
        out_specs=P(None, None, "band", "chan", None),
        check_vma=False,
    )
```

```python
import math

import jax
import jax.numpy as jnp
from jax import lax
from jax.sharding import PartitionSpec as P

DEC = 10
TAPS = 63
W = 256
NF = 128
HALF = 32


def mean_matrix(length, half):
    rows = jnp.arange(length, dtype=jnp.int32)[:, None]
    cols = jnp.arange(length, dtype=jnp.int32)[None, :]
    begins = jnp.clip(cols - half, 0, length - 2 * half - 1)
    inside = (rows >= begins) & (rows <= begins + 2 * half)
    return inside.astype(jnp.float32)


def dft_table(length, bins):
    samples = jnp.arange(length, dtype=jnp.int32)[:, None]
    freqs = jnp.arange(bins, dtype=jnp.int32)[None, :]
    phase = samples * freqs % length
    angle = phase.astype(jnp.float32) * (2.0 * math.pi / length)
    return jnp.concatenate([jnp.cos(angle), -jnp.sin(angle)], axis=1)


def filter_table(taps, phases):
    padded = jnp.pad(taps, (0, phases * DEC - TAPS))
    grid = padded.reshape(phases, DEC)
    rows = jnp.arange(W + phases - 1, dtype=jnp.int32)[:, None]
    cols = jnp.arange(W, dtype=jnp.int32)[None, :]
    onehot = (
        (rows - cols)[None, :, :] == jnp.arange(phases, dtype=jnp.int32)[:, None, None]
    ).astype(jnp.bfloat16)
    table = jnp.einsum("jqn,jr->qrn", onehot, grid, preferred_element_type=jnp.float32)
    return table.reshape((W + phases - 1) * DEC, W).astype(jnp.bfloat16)


def window_spectrum(segment, offset, table, level_matrix, transform):
    span = table.shape[0]
    piece = lax.dynamic_slice_in_dim(segment, offset, span, 1)
    decimated = jnp.dot(piece, table, preferred_element_type=jnp.float32)
    level = jnp.dot(jnp.abs(decimated), level_matrix, precision=lax.Precision.HIGHEST) / (
        2 * HALF + 1
    )
    normed = decimated / (level + 1e-05)
    spectrum = lax.dot_general(
        transform, normed, (((0,), (1,)), ((), ())), precision=lax.Precision.HIGHEST
    )
    return spectrum.reshape(2, NF, segment.shape[0]).astype(jnp.bfloat16)


def body(raw, offsets, taps, partner):
    phases = (TAPS + DEC - 1) // DEC
    table = filter_table(taps, phases)
    level_matrix = mean_matrix(W, HALF)
    transform = dft_table(W, NF)
    spectrum = window_spectrum(raw[0], offsets[0], table, level_matrix, transform)
    chan_count = lax.axis_size("chan")
    band_count = lax.axis_size("band")
    part_count, bin_count, channel_count = spectrum.shape
    bins = bin_count // band_count
    width = channel_count // chan_count
    arranged = spectrum.reshape(part_count, band_count, bins, chan_count, width)
    arranged = arranged.transpose(0, 2, 4, 3, 1).reshape(
        part_count, bins, width, chan_count * band_count
    )
    local = lax.all_to_all(arranged, ("chan", "band"), split_axis=3, concat_axis=3, tiled=True)

    def exchange(rows, number):
        def branch(shift):
            pairs = [(a, a ^ shift) for a in range(chan_count)]
            return lambda x: lax.ppermute(x, "chan", pairs)

        branches = [branch(shift) for shift in range(1, chan_count)]
        return lax.switch(number - 1, branches, rows)

    first_other = exchange(local, partner[0, 0])
    second_other = exchange(local, partner[1, 0])
    factor = 1.0 / (W * math.sqrt(local.shape[3]))
    columns = []
    for other_rows in (first_other, second_other):
        columns.append(other_rows)
        columns.append(jnp.stack([-other_rows[1], other_rows[0]]))
    mixed = jnp.stack(columns)
    own = jnp.broadcast_to(local[None], mixed.shape)
    product = jnp.einsum("qpfiw,qpfjw->qfij", own, mixed, preferred_element_type=jnp.float32)
    return (product * factor).reshape(2, 2, bins, width, width)


def solution(mesh):
    return jax.shard_map(
        body,
        mesh=mesh,
        in_specs=(P(("chan", "band"), None, None), P(("chan", "band")), P(), P()),
        out_specs=P(None, None, "band", "chan", None),
        check_vma=False,
    )
```

```python
import math

import jax
import jax.numpy as jnp
from jax import lax
from jax.sharding import PartitionSpec as P

DEC = 10
TAPS = 63
W = 256
NF = 128
HALF = 32


def mean_matrix(length, half):
    rows = jnp.arange(length, dtype=jnp.int32)[:, None]
    cols = jnp.arange(length, dtype=jnp.int32)[None, :]
    begins = jnp.clip(cols - half, 0, length - 2 * half - 1)
    inside = (rows >= begins) & (rows <= begins + 2 * half)
    return inside.astype(jnp.float32)


def dft_table(length, bins):
    samples = jnp.arange(length, dtype=jnp.int32)[:, None]
    freqs = jnp.arange(bins, dtype=jnp.int32)[None, :]
    phase = samples * freqs % length
    angle = phase.astype(jnp.float32) * (2.0 * math.pi / length)
    return jnp.concatenate([jnp.cos(angle), -jnp.sin(angle)], axis=1)


def filter_table(taps, phases):
    padded = jnp.pad(taps, (0, phases * DEC - TAPS))
    grid = padded.reshape(phases, DEC)
    rows = jnp.arange(W + phases - 1, dtype=jnp.int32)[:, None]
    cols = jnp.arange(W, dtype=jnp.int32)[None, :]
    onehot = (
        (rows - cols)[None, :, :] == jnp.arange(phases, dtype=jnp.int32)[:, None, None]
    ).astype(jnp.bfloat16)
    table = jnp.einsum("jqn,jr->qrn", onehot, grid, preferred_element_type=jnp.float32)
    return table.reshape((W + phases - 1) * DEC, W).astype(jnp.bfloat16)


def window_spectrum(segment, offset, table, level_matrix, transform, blocks, bands):
    span = table.shape[0]
    half = W // 2
    rows = span - half * DEC
    decimated = jnp.concatenate(
        [
            jnp.dot(
                lax.dynamic_slice_in_dim(segment, offset + start * DEC, rows, 1),
                table[start * DEC : start * DEC + rows, start : start + half],
                preferred_element_type=jnp.float32,
            )
            for start in (0, half)
        ],
        axis=1,
    )
    level = jnp.dot(jnp.abs(decimated), level_matrix, precision=lax.Precision.HIGHEST) / (
        2 * HALF + 1
    )
    normed = decimated / (level + 1e-05)
    channels = segment.shape[0]
    ordered = transform.reshape(W, 2, bands, NF // bands).transpose(0, 2, 1, 3).reshape(W, 2 * NF)
    spectrum = jnp.einsum(
        "ain,nk->aki",
        normed.reshape(blocks, channels // blocks, W),
        ordered,
        precision=lax.Precision.HIGHEST,
    )
    return spectrum.reshape(blocks, bands, 2, NF // bands, channels // blocks).astype(jnp.bfloat16)


def body(raw, offsets, taps, partner):
    phases = (TAPS + DEC - 1) // DEC
    table = filter_table(taps, phases)
    level_matrix = mean_matrix(W, HALF)
    transform = dft_table(W, NF)
    chan_count = lax.axis_size("chan")
    band_count = lax.axis_size("band")
    spectrum = window_spectrum(
        raw[0], offsets[0], table, level_matrix, transform, chan_count, band_count
    )
    _, _, part_count, bins, width = spectrum.shape
    arranged = spectrum.transpose(2, 3, 4, 0, 1).reshape(
        part_count, bins, width, chan_count * band_count
    )
    local = lax.all_to_all(arranged, ("chan", "band"), split_axis=3, concat_axis=3, tiled=True)

    def exchange(rows, number):
        def branch(shift):
            pairs = [(a, a ^ shift) for a in range(chan_count)]
            return lambda x: lax.ppermute(x, "chan", pairs)

        branches = [branch(shift) for shift in range(1, chan_count)]
        return lax.switch(number - 1, branches, rows)

    first_other = exchange(local, partner[0, 0])
    second_other = exchange(local, partner[1, 0])
    factor = 1.0 / (W * math.sqrt(local.shape[3]))
    columns = []
    for other_rows in (first_other, second_other):
        columns.append(other_rows)
        columns.append(jnp.stack([-other_rows[1], other_rows[0]]))
    mixed = jnp.stack(columns)
    own = jnp.broadcast_to(local[None], mixed.shape)
    product = jnp.einsum("qpfiw,qpfjw->qfij", own, mixed, preferred_element_type=jnp.float32)
    return (product * factor).reshape(2, 2, bins, width, width)


def solution(mesh):
    return jax.shard_map(
        body,
        mesh=mesh,
        in_specs=(P(("chan", "band"), None, None), P(("chan", "band")), P(), P()),
        out_specs=P(None, None, "band", "chan", None),
        check_vma=False,
    )
```

```python
import math

import jax
import jax.numpy as jnp
from jax import lax
from jax.sharding import PartitionSpec as P

DEC = 10
TAPS = 63
W = 256
NF = 128
HALF = 32


def mean_matrix(length, half):
    rows = jnp.arange(length, dtype=jnp.int32)[:, None]
    cols = jnp.arange(length, dtype=jnp.int32)[None, :]
    begins = jnp.clip(cols - half, 0, length - 2 * half - 1)
    inside = (rows >= begins) & (rows <= begins + 2 * half)
    return inside.astype(jnp.float32)


def dft_table(length, bins):
    samples = jnp.arange(length, dtype=jnp.int32)[:, None]
    freqs = jnp.arange(bins, dtype=jnp.int32)[None, :]
    phase = samples * freqs % length
    angle = phase.astype(jnp.float32) * (2.0 * math.pi / length)
    return jnp.concatenate([jnp.cos(angle), -jnp.sin(angle)], axis=1)


def filter_table(taps, phases):
    padded = jnp.pad(taps, (0, phases * DEC - TAPS))
    grid = padded.reshape(phases, DEC)
    rows = jnp.arange(W + phases - 1, dtype=jnp.int32)[:, None]
    cols = jnp.arange(W, dtype=jnp.int32)[None, :]
    onehot = (
        (rows - cols)[None, :, :] == jnp.arange(phases, dtype=jnp.int32)[:, None, None]
    ).astype(jnp.bfloat16)
    table = jnp.einsum("jqn,jr->qrn", onehot, grid, preferred_element_type=jnp.float32)
    return table.reshape((W + phases - 1) * DEC, W).astype(jnp.bfloat16)


def window_spectrum(segment, offset, table, level_matrix, transform):
    span = table.shape[0]
    piece = lax.dynamic_slice_in_dim(segment, offset, span, 1)
    decimated = jnp.dot(piece, table, preferred_element_type=jnp.float32)
    level = jnp.dot(jnp.abs(decimated), level_matrix, precision=lax.Precision.HIGHEST) / (
        2 * HALF + 1
    )
    normed = decimated / (level + 1e-05)
    spectrum = lax.dot_general(
        transform, normed, (((0,), (1,)), ((), ())), precision=lax.Precision.HIGHEST
    )
    return spectrum.reshape(2, NF, segment.shape[0]).astype(jnp.bfloat16)


def body(raw, offsets, taps, partner):
    phases = (TAPS + DEC - 1) // DEC
    table = filter_table(taps, phases)
    level_matrix = mean_matrix(W, HALF)
    transform = dft_table(W, NF)
    spectrum = window_spectrum(raw[0], offsets[0], table, level_matrix, transform)
    chan_count = lax.axis_size("chan")
    band_count = lax.axis_size("band")
    part_count, bin_count, channel_count = spectrum.shape
    bins = bin_count // band_count
    width = channel_count // chan_count
    arranged = spectrum.reshape(part_count, band_count, bins, chan_count, width)
    arranged = arranged.transpose(0, 2, 4, 3, 1).reshape(
        part_count, bins, width, chan_count * band_count
    )
    halves = [
        lax.all_to_all(arranged[part : part + 1], ("chan", "band"), 3, 3, tiled=True)
        for part in range(part_count)
    ]

    def exchange(rows, number):
        def branch(shift):
            pairs = [(a, a ^ shift) for a in range(chan_count)]
            return lambda x: lax.ppermute(x, "chan", pairs)

        branches = [branch(shift) for shift in range(1, chan_count)]
        return lax.switch(number - 1, branches, rows)

    others = [[exchange(rows, partner[r, 0]) for rows in halves] for r in range(2)]
    local = jnp.concatenate(halves)
    first_other = jnp.concatenate(others[0])
    second_other = jnp.concatenate(others[1])
    factor = 1.0 / (W * math.sqrt(local.shape[3]))
    columns = []
    for other_rows in (first_other, second_other):
        columns.append(other_rows)
        columns.append(jnp.stack([-other_rows[1], other_rows[0]]))
    mixed = jnp.stack(columns)
    own = jnp.broadcast_to(local[None], mixed.shape)
    product = jnp.einsum("qpfiw,qpfjw->qfij", own, mixed, preferred_element_type=jnp.float32)
    return (product * factor).reshape(2, 2, bins, width, width)


def solution(mesh):
    return jax.shard_map(
        body,
        mesh=mesh,
        in_specs=(P(("chan", "band"), None, None), P(("chan", "band")), P(), P()),
        out_specs=P(None, None, "band", "chan", None),
        check_vma=False,
    )
```

```python
import math

import jax
import jax.numpy as jnp
from jax import lax
from jax.sharding import PartitionSpec as P

DEC = 10
TAPS = 63
W = 256
NF = 128
HALF = 32


def mean_matrix(length, half):
    rows = jnp.arange(length, dtype=jnp.int32)[:, None]
    cols = jnp.arange(length, dtype=jnp.int32)[None, :]
    begins = jnp.clip(cols - half, 0, length - 2 * half - 1)
    inside = (rows >= begins) & (rows <= begins + 2 * half)
    return inside.astype(jnp.float32)


def dft_table(length, bins):
    samples = jnp.arange(length, dtype=jnp.int32)[:, None]
    freqs = jnp.arange(bins, dtype=jnp.int32)[None, :]
    phase = samples * freqs % length
    angle = phase.astype(jnp.float32) * (2.0 * math.pi / length)
    return jnp.concatenate([jnp.cos(angle), -jnp.sin(angle)], axis=1)


def filter_table(taps, phases):
    padded = jnp.pad(taps, (0, phases * DEC - TAPS))
    grid = padded.reshape(phases, DEC)
    rows = jnp.arange(W + phases - 1, dtype=jnp.int32)[:, None]
    cols = jnp.arange(W, dtype=jnp.int32)[None, :]
    onehot = (
        (rows - cols)[None, :, :] == jnp.arange(phases, dtype=jnp.int32)[:, None, None]
    ).astype(jnp.bfloat16)
    table = jnp.einsum("jqn,jr->qrn", onehot, grid, preferred_element_type=jnp.float32)
    return table.reshape((W + phases - 1) * DEC, W).astype(jnp.bfloat16)


def window_spectrum(segment, offset, table, level_matrix, transform, blocks, bands):
    span = table.shape[0]
    piece = lax.dynamic_slice_in_dim(segment, offset, span, 1)
    decimated = jnp.dot(piece, table, preferred_element_type=jnp.float32)
    level = jnp.dot(jnp.abs(decimated), level_matrix, precision=lax.Precision.HIGHEST) / (
        2 * HALF + 1
    )
    normed = decimated / (level + 1e-05)
    channels = segment.shape[0]
    ordered = transform.reshape(W, 2, bands, NF // bands).transpose(2, 1, 3, 0).reshape(2 * NF, W)
    spectrum = jnp.einsum(
        "akn,ain->aki",
        jnp.broadcast_to(ordered[None], (blocks, 2 * NF, W)),
        normed.reshape(blocks, channels // blocks, W),
        precision=lax.Precision.HIGHEST,
    )
    return spectrum.reshape(blocks, bands, 2, NF // bands, channels // blocks).astype(jnp.bfloat16)


def body(raw, offsets, taps, partner):
    phases = (TAPS + DEC - 1) // DEC
    table = filter_table(taps, phases)
    level_matrix = mean_matrix(W, HALF)
    transform = dft_table(W, NF)
    chan_count = lax.axis_size("chan")
    band_count = lax.axis_size("band")
    spectrum = window_spectrum(
        raw[0], offsets[0], table, level_matrix, transform, chan_count, band_count
    )
    _, _, part_count, bins, width = spectrum.shape
    arranged = spectrum.transpose(2, 3, 4, 0, 1).reshape(
        part_count, bins, width, chan_count * band_count
    )
    local = lax.all_to_all(arranged, ("chan", "band"), split_axis=3, concat_axis=3, tiled=True)

    def exchange(rows, number):
        def branch(shift):
            pairs = [(a, a ^ shift) for a in range(chan_count)]
            return lambda x: lax.ppermute(x, "chan", pairs)

        branches = [branch(shift) for shift in range(1, chan_count)]
        return lax.switch(number - 1, branches, rows)

    first_other = exchange(local, partner[0, 0])
    second_other = exchange(local, partner[1, 0])
    factor = 1.0 / (W * math.sqrt(local.shape[3]))
    columns = []
    for other_rows in (first_other, second_other):
        columns.append(other_rows)
        columns.append(jnp.stack([-other_rows[1], other_rows[0]]))
    mixed = jnp.stack(columns)
    own = jnp.broadcast_to(local[None], mixed.shape)
    product = jnp.einsum("qpfiw,qpfjw->qfij", own, mixed, preferred_element_type=jnp.float32)
    return (product * factor).reshape(2, 2, bins, width, width)


def solution(mesh):
    return jax.shard_map(
        body,
        mesh=mesh,
        in_specs=(P(("chan", "band"), None, None), P(("chan", "band")), P(), P()),
        out_specs=P(None, None, "band", "chan", None),
        check_vma=False,
    )
```

```python
import math

import jax
import jax.numpy as jnp
from jax import lax
from jax.sharding import PartitionSpec as P

DEC = 10
TAPS = 63
W = 256
NF = 128
HALF = 32


def mean_matrix(length, half):
    rows = jnp.arange(length, dtype=jnp.int32)[:, None]
    cols = jnp.arange(length, dtype=jnp.int32)[None, :]
    begins = jnp.clip(cols - half, 0, length - 2 * half - 1)
    inside = (rows >= begins) & (rows <= begins + 2 * half)
    return inside.astype(jnp.float32)


def dft_table(length, bins):
    samples = jnp.arange(length, dtype=jnp.int32)[:, None]
    freqs = jnp.arange(bins, dtype=jnp.int32)[None, :]
    phase = samples * freqs % length
    angle = phase.astype(jnp.float32) * (2.0 * math.pi / length)
    return jnp.concatenate([jnp.cos(angle), -jnp.sin(angle)], axis=1)


def filter_table(taps, phases):
    padded = jnp.pad(taps, (0, phases * DEC - TAPS))
    grid = padded.reshape(phases, DEC)
    rows = jnp.arange(W + phases - 1, dtype=jnp.int32)[:, None]
    cols = jnp.arange(W, dtype=jnp.int32)[None, :]
    onehot = (
        (rows - cols)[None, :, :] == jnp.arange(phases, dtype=jnp.int32)[:, None, None]
    ).astype(jnp.bfloat16)
    table = jnp.einsum("jqn,jr->qrn", onehot, grid, preferred_element_type=jnp.float32)
    return table.reshape((W + phases - 1) * DEC, W).astype(jnp.bfloat16)


def window_spectrum(segment, offset, table, level_matrix, transform, blocks, bands):
    span = table.shape[0]
    piece = lax.dynamic_slice_in_dim(segment, offset, span, 1)
    decimated = jnp.dot(piece, table, preferred_element_type=jnp.float32)
    level = jnp.dot(jnp.abs(decimated), level_matrix, precision=lax.Precision.HIGHEST) / (
        2 * HALF + 1
    )
    normed = decimated / (level + 1e-05)
    channels = segment.shape[0]
    ordered = transform.reshape(W, 2, bands, NF // bands).transpose(2, 1, 3, 0).reshape(2 * NF, W)
    spectrum = jnp.einsum(
        "akn,ain->aki",
        jnp.broadcast_to(ordered[None], (blocks, 2 * NF, W)),
        normed.reshape(blocks, channels // blocks, W),
        precision=lax.Precision.HIGHEST,
    )
    return spectrum.reshape(blocks, bands, 2, NF // bands, channels // blocks).astype(jnp.bfloat16)


def body(raw, offsets, taps, partner):
    phases = (TAPS + DEC - 1) // DEC
    table = filter_table(taps, phases)
    level_matrix = mean_matrix(W, HALF)
    transform = dft_table(W, NF)
    chan_count = lax.axis_size("chan")
    band_count = lax.axis_size("band")
    spectrum = window_spectrum(
        raw[0], offsets[0], table, level_matrix, transform, chan_count, band_count
    )
    _, _, part_count, bins, width = spectrum.shape
    arranged = spectrum.transpose(2, 3, 4, 0, 1).reshape(
        part_count, bins, width, chan_count * band_count
    )
    local = lax.all_to_all(arranged, ("chan", "band"), split_axis=3, concat_axis=3, tiled=True)

    def exchange(rows, number):
        def branch(shift):
            pairs = [(a, a ^ shift) for a in range(chan_count)]
            return lambda x: lax.ppermute(x, "chan", pairs)

        branches = [branch(shift) for shift in range(1, chan_count)]
        return lax.switch(number - 1, branches, rows)

    first_other = exchange(local, partner[0, 0])
    second_other = exchange(local, partner[1, 0])
    factor = 1.0 / (W * math.sqrt(local.shape[3]))
    variants = jnp.stack([local, jnp.stack([local[1], -local[0]])])
    rounds = jnp.stack([first_other, second_other])
    own = jnp.broadcast_to(variants[None], (2,) + variants.shape)
    mixed = jnp.broadcast_to(rounds[:, None], (2, 2) + rounds.shape[1:])
    product = jnp.einsum("rqpfiw,rqpfjw->rqfij", own, mixed, preferred_element_type=jnp.float32)
    return (product * factor).reshape(2, 2, bins, width, width)


def solution(mesh):
    return jax.shard_map(
        body,
        mesh=mesh,
        in_specs=(P(("chan", "band"), None, None), P(("chan", "band")), P(), P()),
        out_specs=P(None, None, "band", "chan", None),
        check_vma=False,
    )
```

```python
import math

import jax
import jax.numpy as jnp
from jax import lax
from jax.sharding import PartitionSpec as P

DEC = 10
TAPS = 63
W = 256
NF = 128
HALF = 32


def mean_matrix(length, half):
    rows = jnp.arange(length, dtype=jnp.int32)[:, None]
    cols = jnp.arange(length, dtype=jnp.int32)[None, :]
    begins = jnp.clip(cols - half, 0, length - 2 * half - 1)
    inside = (rows >= begins) & (rows <= begins + 2 * half)
    return inside.astype(jnp.float32)


def dft_table(length, bins):
    samples = jnp.arange(length, dtype=jnp.int32)[:, None]
    freqs = jnp.arange(bins, dtype=jnp.int32)[None, :]
    phase = samples * freqs % length
    angle = phase.astype(jnp.float32) * (2.0 * math.pi / length)
    return jnp.concatenate([jnp.cos(angle), -jnp.sin(angle)], axis=1)


def filter_table(taps, phases):
    padded = jnp.pad(taps, (0, phases * DEC - TAPS))
    grid = padded.reshape(phases, DEC)
    rows = jnp.arange(W + phases - 1, dtype=jnp.int32)[:, None]
    cols = jnp.arange(W, dtype=jnp.int32)[None, :]
    onehot = (
        (rows - cols)[None, :, :] == jnp.arange(phases, dtype=jnp.int32)[:, None, None]
    ).astype(jnp.bfloat16)
    table = jnp.einsum("jqn,jr->qrn", onehot, grid, preferred_element_type=jnp.float32)
    return table.reshape((W + phases - 1) * DEC, W).astype(jnp.bfloat16)


def window_spectrum(segment, offset, table, level_matrix, transform, blocks, bands):
    span = table.shape[0]
    piece = lax.dynamic_slice_in_dim(segment, offset, span, 1)
    decimated = jnp.dot(piece, table, preferred_element_type=jnp.float32)
    level = jnp.dot(jnp.abs(decimated), level_matrix, precision=lax.Precision.HIGHEST) / (
        2 * HALF + 1
    )
    normed = decimated / (level + 1e-05)
    channels = segment.shape[0]
    ordered = transform.reshape(W, 2, bands, NF // bands).transpose(2, 1, 3, 0).reshape(2 * NF, W)
    spectrum = jnp.einsum(
        "akn,ain->aki",
        jnp.broadcast_to(ordered[None], (blocks, 2 * NF, W)),
        normed.reshape(blocks, channels // blocks, W),
        precision=lax.Precision.HIGHEST,
    )
    return spectrum.reshape(blocks, bands, 2, NF // bands, channels // blocks).astype(jnp.bfloat16)


def body(raw, offsets, taps, partner):
    phases = (TAPS + DEC - 1) // DEC
    table = filter_table(taps, phases)
    level_matrix = mean_matrix(W, HALF)
    transform = dft_table(W, NF)
    chan_count = lax.axis_size("chan")
    band_count = lax.axis_size("band")
    spectrum = window_spectrum(
        raw[0], offsets[0], table, level_matrix, transform, chan_count, band_count
    )
    _, _, part_count, bins, width = spectrum.shape
    arranged = spectrum.transpose(2, 3, 4, 0, 1).reshape(
        part_count, bins, width, chan_count * band_count
    )
    local = lax.all_to_all(arranged, ("chan", "band"), split_axis=3, concat_axis=3, tiled=True)

    factor = 1.0 / (W * math.sqrt(local.shape[3]))

    def cross(own_rows, other_rows):
        mixed = jnp.stack([other_rows, jnp.stack([-other_rows[1], other_rows[0]])])
        own = jnp.broadcast_to(own_rows[None], mixed.shape)
        product = jnp.einsum("qpfiw,qpfjw->qfij", own, mixed, preferred_element_type=jnp.float32)
        return product * factor

    def branch(shift, work):
        pairs = [(a, a ^ shift) for a in range(chan_count)]
        return lambda x, y: (lax.ppermute(x, "chan", pairs), work(x, y))

    def exchange(number, work, rows, earlier):
        branches = [branch(shift, work) for shift in range(1, chan_count)]
        return lax.switch(number - 1, branches, rows, earlier)

    first_other, _ = exchange(partner[0, 0], lambda x, y: y, local, local)
    second_other, first_cross = exchange(partner[1, 0], cross, local, first_other)
    second_cross = cross(local, second_other)
    return jnp.stack([first_cross, second_cross])


def solution(mesh):
    return jax.shard_map(
        body,
        mesh=mesh,
        in_specs=(P(("chan", "band"), None, None), P(("chan", "band")), P(), P()),
        out_specs=P(None, None, "band", "chan", None),
        check_vma=False,
    )
```

```python
import math

import jax
import jax.numpy as jnp
from jax import lax
from jax.sharding import PartitionSpec as P

DEC = 10
TAPS = 63
W = 256
NF = 128
HALF = 32


def mean_matrix(length, half):
    rows = jnp.arange(length, dtype=jnp.int32)[:, None]
    cols = jnp.arange(length, dtype=jnp.int32)[None, :]
    begins = jnp.clip(cols - half, 0, length - 2 * half - 1)
    inside = (rows >= begins) & (rows <= begins + 2 * half)
    return inside.astype(jnp.float32)


def dft_table(length, bins):
    samples = jnp.arange(length, dtype=jnp.int32)[:, None]
    freqs = jnp.arange(bins, dtype=jnp.int32)[None, :]
    phase = samples * freqs % length
    angle = phase.astype(jnp.float32) * (2.0 * math.pi / length)
    return jnp.concatenate([jnp.cos(angle), -jnp.sin(angle)], axis=1)


def filter_table(taps, phases):
    padded = jnp.pad(taps, (0, phases * DEC - TAPS))
    grid = padded.reshape(phases, DEC)
    rows = jnp.arange(W + phases - 1, dtype=jnp.int32)[:, None]
    cols = jnp.arange(W, dtype=jnp.int32)[None, :]
    onehot = (
        (rows - cols)[None, :, :] == jnp.arange(phases, dtype=jnp.int32)[:, None, None]
    ).astype(jnp.bfloat16)
    table = jnp.einsum("jqn,jr->qrn", onehot, grid, preferred_element_type=jnp.float32)
    return table.reshape((W + phases - 1) * DEC, W).astype(jnp.bfloat16)


def window_spectrum(segment, offset, table, level_matrix, transform, blocks, bands):
    span = table.shape[0]
    piece = lax.dynamic_slice_in_dim(segment, offset, span, 1)
    decimated = jnp.dot(piece, table, preferred_element_type=jnp.float32)
    level = jnp.dot(jnp.abs(decimated), level_matrix, precision=lax.Precision.HIGHEST) / (
        2 * HALF + 1
    )
    normed = decimated / (level + 1e-05)
    channels = segment.shape[0]
    ordered = transform.reshape(W, 2, bands, NF // bands).transpose(2, 1, 3, 0).reshape(2 * NF, W)
    spectrum = jnp.einsum(
        "akn,ain->aki",
        jnp.broadcast_to(ordered[None], (blocks, 2 * NF, W)),
        normed.reshape(blocks, channels // blocks, W),
        precision=lax.Precision.HIGHEST,
    )
    return spectrum.reshape(blocks, bands, 2, NF // bands, channels // blocks).astype(jnp.bfloat16)


def body(raw, offsets, taps, partner):
    phases = (TAPS + DEC - 1) // DEC
    table = filter_table(taps, phases)
    level_matrix = mean_matrix(W, HALF)
    transform = dft_table(W, NF)
    chan_count = lax.axis_size("chan")
    band_count = lax.axis_size("band")
    spectrum = window_spectrum(
        raw[0], offsets[0], table, level_matrix, transform, chan_count, band_count
    )
    _, _, part_count, bins, width = spectrum.shape
    arranged = spectrum.transpose(2, 3, 4, 1, 0).reshape(
        part_count, bins, width, chan_count * band_count
    )
    local = lax.all_to_all(arranged, ("band", "chan"), split_axis=3, concat_axis=3, tiled=True)

    def exchange(rows, number):
        def branch(shift):
            pairs = [(a, a ^ shift) for a in range(chan_count)]
            return lambda x: lax.ppermute(x, "chan", pairs)

        branches = [branch(shift) for shift in range(1, chan_count)]
        return lax.switch(number - 1, branches, rows)

    first_other = exchange(local, partner[0, 0])
    second_other = exchange(local, partner[1, 0])
    factor = 1.0 / (W * math.sqrt(local.shape[3]))
    columns = []
    for other_rows in (first_other, second_other):
        columns.append(other_rows)
        columns.append(jnp.stack([-other_rows[1], other_rows[0]]))
    mixed = jnp.stack(columns)
    own = jnp.broadcast_to(local[None], mixed.shape)
    product = jnp.einsum("qpfiw,qpfjw->qfij", own, mixed, preferred_element_type=jnp.float32)
    return (product * factor).reshape(2, 2, bins, width, width)


def solution(mesh):
    return jax.shard_map(
        body,
        mesh=mesh,
        in_specs=(P(("chan", "band"), None, None), P(("chan", "band")), P(), P()),
        out_specs=P(None, None, "band", "chan", None),
        check_vma=False,
    )
```

```python
import math

import jax
import jax.numpy as jnp
from jax import lax
from jax.sharding import PartitionSpec as P

DEC = 10
TAPS = 63
W = 256
NF = 128
HALF = 32


def mean_matrix(length, half):
    rows = jnp.arange(length, dtype=jnp.int32)[:, None]
    cols = jnp.arange(length, dtype=jnp.int32)[None, :]
    begins = jnp.clip(cols - half, 0, length - 2 * half - 1)
    inside = (rows >= begins) & (rows <= begins + 2 * half)
    return inside.astype(jnp.float32)


def dft_table(length, bins):
    samples = jnp.arange(length, dtype=jnp.int32)[:, None]
    freqs = jnp.arange(bins, dtype=jnp.int32)[None, :]
    phase = samples * freqs % length
    angle = phase.astype(jnp.float32) * (2.0 * math.pi / length)
    return jnp.concatenate([jnp.cos(angle), -jnp.sin(angle)], axis=1)


def filter_table(taps, phases):
    padded = jnp.pad(taps, (0, phases * DEC - TAPS))
    grid = padded.reshape(phases, DEC)
    rows = jnp.arange(W + phases - 1, dtype=jnp.int32)[:, None]
    cols = jnp.arange(W, dtype=jnp.int32)[None, :]
    onehot = (
        (rows - cols)[None, :, :] == jnp.arange(phases, dtype=jnp.int32)[:, None, None]
    ).astype(jnp.bfloat16)
    table = jnp.einsum("jqn,jr->qrn", onehot, grid, preferred_element_type=jnp.float32)
    return table.reshape((W + phases - 1) * DEC, W).astype(jnp.bfloat16)


def window_spectrum(segment, offset, table, level_matrix, transform, blocks, bands):
    span = table.shape[0]
    piece = lax.dynamic_slice_in_dim(segment, offset, span, 1)
    decimated = jnp.dot(piece, table, preferred_element_type=jnp.float32)
    level = jnp.dot(jnp.abs(decimated), level_matrix, precision=lax.Precision.HIGH) / (
        2 * HALF + 1
    )
    normed = decimated / (level + 1e-05)
    channels = segment.shape[0]
    ordered = transform.reshape(W, 2, bands, NF // bands).transpose(2, 1, 3, 0).reshape(2 * NF, W)
    spectrum = jnp.einsum(
        "akn,ain->aki",
        jnp.broadcast_to(ordered[None], (blocks, 2 * NF, W)),
        normed.reshape(blocks, channels // blocks, W),
        precision=lax.Precision.HIGH,
    )
    return spectrum.reshape(blocks, bands, 2, NF // bands, channels // blocks).astype(jnp.bfloat16)


def body(raw, offsets, taps, partner):
    phases = (TAPS + DEC - 1) // DEC
    table = filter_table(taps, phases)
    level_matrix = mean_matrix(W, HALF)
    transform = dft_table(W, NF)
    chan_count = lax.axis_size("chan")
    band_count = lax.axis_size("band")
    spectrum = window_spectrum(
        raw[0], offsets[0], table, level_matrix, transform, chan_count, band_count
    )
    _, _, part_count, bins, width = spectrum.shape
    arranged = spectrum.transpose(2, 3, 4, 0, 1).reshape(
        part_count, bins, width, chan_count * band_count
    )
    local = lax.all_to_all(arranged, ("chan", "band"), split_axis=3, concat_axis=3, tiled=True)

    def exchange(rows, number):
        def branch(shift):
            pairs = [(a, a ^ shift) for a in range(chan_count)]
            return lambda x: lax.ppermute(x, "chan", pairs)

        branches = [branch(shift) for shift in range(1, chan_count)]
        return lax.switch(number - 1, branches, rows)

    first_other = exchange(local, partner[0, 0])
    second_other = exchange(local, partner[1, 0])
    factor = 1.0 / (W * math.sqrt(local.shape[3]))
    columns = []
    for other_rows in (first_other, second_other):
        columns.append(other_rows)
        columns.append(jnp.stack([-other_rows[1], other_rows[0]]))
    mixed = jnp.stack(columns)
    own = jnp.broadcast_to(local[None], mixed.shape)
    product = jnp.einsum("qpfiw,qpfjw->qfij", own, mixed, preferred_element_type=jnp.float32)
    return (product * factor).reshape(2, 2, bins, width, width)


def solution(mesh):
    return jax.shard_map(
        body,
        mesh=mesh,
        in_specs=(P(("chan", "band"), None, None), P(("chan", "band")), P(), P()),
        out_specs=P(None, None, "band", "chan", None),
        check_vma=False,
    )
```

```python
import math

import jax
import jax.numpy as jnp
from jax import lax
from jax.sharding import PartitionSpec as P

DEC = 10
TAPS = 63
W = 256
NF = 128
HALF = 32


def mean_matrix(length, half):
    rows = jnp.arange(length, dtype=jnp.int32)[:, None]
    cols = jnp.arange(length, dtype=jnp.int32)[None, :]
    begins = jnp.clip(cols - half, 0, length - 2 * half - 1)
    inside = (rows >= begins) & (rows <= begins + 2 * half)
    return inside.astype(jnp.float32)


def dft_table(length, bins):
    samples = jnp.arange(length, dtype=jnp.int32)[:, None]
    freqs = jnp.arange(bins, dtype=jnp.int32)[None, :]
    phase = samples * freqs % length
    angle = phase.astype(jnp.float32) * (2.0 * math.pi / length)
    return jnp.concatenate([jnp.cos(angle), -jnp.sin(angle)], axis=1)


def filter_table(taps, phases):
    padded = jnp.pad(taps, (0, phases * DEC - TAPS))
    grid = padded.reshape(phases, DEC)
    rows = jnp.arange(W + phases - 1, dtype=jnp.int32)[:, None]
    cols = jnp.arange(W, dtype=jnp.int32)[None, :]
    onehot = (
        (rows - cols)[None, :, :] == jnp.arange(phases, dtype=jnp.int32)[:, None, None]
    ).astype(jnp.bfloat16)
    table = jnp.einsum("jqn,jr->qrn", onehot, grid, preferred_element_type=jnp.float32)
    return table.reshape((W + phases - 1) * DEC, W).astype(jnp.bfloat16)


def window_spectrum(segment, offset, table, level_matrix, transform, blocks, bands):
    span = table.shape[0]
    channels = segment.shape[0]
    ordered = transform.reshape(W, 2, bands, NF // bands).transpose(2, 1, 3, 0).reshape(2 * NF, W)
    half = W // 2
    rows = span - half * DEC
    pieces = [
        jnp.dot(
            lax.dynamic_slice_in_dim(segment, offset + start * DEC, rows, 1),
            table[start * DEC : start * DEC + rows, start : start + half],
            preferred_element_type=jnp.float32,
        )
        for start in (0, half)
    ]
    level = sum(
        jnp.dot(jnp.abs(piece), level_matrix[start : start + half], precision=lax.Precision.HIGH)
        for piece, start in zip(pieces, (0, half))
    ) / (2 * HALF + 1)
    spectrum = sum(
        jnp.einsum(
            "akn,ain->aki",
            jnp.broadcast_to(ordered[None, :, start : start + half], (blocks, 2 * NF, half)),
            (piece / (level + 1e-05)[:, start : start + half]).reshape(blocks, channels // blocks, half),
            precision=lax.Precision.HIGH,
        )
        for piece, start in zip(pieces, (0, half))
    )
    return spectrum.reshape(blocks, bands, 2, NF // bands, channels // blocks).astype(jnp.bfloat16)


def body(raw, offsets, taps, partner):
    phases = (TAPS + DEC - 1) // DEC
    table = filter_table(taps, phases)
    level_matrix = mean_matrix(W, HALF)
    transform = dft_table(W, NF)
    chan_count = lax.axis_size("chan")
    band_count = lax.axis_size("band")
    spectrum = window_spectrum(
        raw[0], offsets[0], table, level_matrix, transform, chan_count, band_count
    )
    _, _, part_count, bins, width = spectrum.shape
    arranged = spectrum.transpose(2, 3, 4, 0, 1).reshape(
        part_count, bins, width, chan_count * band_count
    )
    local = lax.all_to_all(arranged, ("chan", "band"), split_axis=3, concat_axis=3, tiled=True)

    def exchange(rows, number):
        def branch(shift):
            pairs = [(a, a ^ shift) for a in range(chan_count)]
            return lambda x: lax.ppermute(x, "chan", pairs)

        branches = [branch(shift) for shift in range(1, chan_count)]
        return lax.switch(number - 1, branches, rows)

    first_other = exchange(local, partner[0, 0])
    second_other = exchange(local, partner[1, 0])
    factor = 1.0 / (W * math.sqrt(local.shape[3]))
    columns = []
    for other_rows in (first_other, second_other):
        columns.append(other_rows)
        columns.append(jnp.stack([-other_rows[1], other_rows[0]]))
    mixed = jnp.stack(columns)
    own = jnp.broadcast_to(local[None], mixed.shape)
    product = jnp.einsum("qpfiw,qpfjw->qfij", own, mixed, preferred_element_type=jnp.float32)
    return (product * factor).reshape(2, 2, bins, width, width)


def solution(mesh):
    return jax.shard_map(
        body,
        mesh=mesh,
        in_specs=(P(("chan", "band"), None, None), P(("chan", "band")), P(), P()),
        out_specs=P(None, None, "band", "chan", None),
        check_vma=False,
    )
```

```python
import math

import jax
import numpy as np
import jax.numpy as jnp
from jax import lax
from jax.sharding import PartitionSpec as P

DEC = 10
TAPS = 63
W = 256
NF = 128
HALF = 32


def mean_matrix(length, half):
    rows = jnp.arange(length, dtype=jnp.int32)[:, None]
    cols = jnp.arange(length, dtype=jnp.int32)[None, :]
    begins = jnp.clip(cols - half, 0, length - 2 * half - 1)
    inside = (rows >= begins) & (rows <= begins + 2 * half)
    return inside.astype(jnp.float32)


def dft_table(length, bins):
    samples = jnp.arange(length, dtype=jnp.int32)[:, None]
    freqs = jnp.arange(bins, dtype=jnp.int32)[None, :]
    phase = samples * freqs % length
    angle = phase.astype(jnp.float32) * (2.0 * math.pi / length)
    return jnp.concatenate([jnp.cos(angle), -jnp.sin(angle)], axis=1)


def filter_table(taps, phases):
    padded = jnp.pad(taps, (0, phases * DEC - TAPS))
    grid = padded.reshape(phases, DEC)
    rows = jnp.arange(W + phases - 1, dtype=jnp.int32)[:, None]
    cols = jnp.arange(W, dtype=jnp.int32)[None, :]
    onehot = (
        (rows - cols)[None, :, :] == jnp.arange(phases, dtype=jnp.int32)[:, None, None]
    ).astype(jnp.bfloat16)
    table = jnp.einsum("jqn,jr->qrn", onehot, grid, preferred_element_type=jnp.float32)
    return table.reshape((W + phases - 1) * DEC, W).astype(jnp.bfloat16)


def window_spectrum(segment, offset, table, level_matrix, transform, blocks, bands):
    span = table.shape[0]
    piece = lax.dynamic_slice_in_dim(segment, offset, span, 1)
    decimated = jnp.dot(piece, table, preferred_element_type=jnp.float32)
    level = jnp.dot(jnp.abs(decimated), level_matrix, precision=lax.Precision.HIGH) / (
        2 * HALF + 1
    )
    normed = decimated / (level + 1e-05)
    channels = segment.shape[0]
    ordered = np.ascontiguousarray(
        transform.reshape(W, 2, bands, NF // bands).transpose(2, 1, 3, 0).reshape(2 * NF, W)
    )
    spectrum = jnp.einsum(
        "akn,ain->aki",
        jnp.broadcast_to(ordered[None], (blocks, 2 * NF, W)),
        normed.reshape(blocks, channels // blocks, W),
        precision=lax.Precision.HIGH,
    )
    return spectrum.reshape(blocks, bands, 2, NF // bands, channels // blocks).astype(jnp.bfloat16)


def body(raw, offsets, taps, partner):
    phases = (TAPS + DEC - 1) // DEC
    table = filter_table(taps, phases)
    rows_np = np.arange(W)[:, None]
    begins_np = np.clip(np.arange(W)[None, :] - HALF, 0, W - 2 * HALF - 1)
    level_matrix = ((rows_np >= begins_np) & (rows_np <= begins_np + 2 * HALF)).astype(np.float32)
    phase = (np.arange(W)[:, None] * np.arange(NF)[None, :]) % W
    angle = phase.astype(np.float32) * np.float32(2.0 * math.pi / W)
    transform = np.concatenate([np.cos(angle), -np.sin(angle)], axis=1).astype(np.float32)
    chan_count = lax.axis_size("chan")
    band_count = lax.axis_size("band")
    spectrum = window_spectrum(
        raw[0], offsets[0], table, level_matrix, transform, chan_count, band_count
    )
    _, _, part_count, bins, width = spectrum.shape
    arranged = spectrum.transpose(2, 3, 4, 0, 1).reshape(
        part_count, bins, width, chan_count * band_count
    )
    local = lax.all_to_all(arranged, ("chan", "band"), split_axis=3, concat_axis=3, tiled=True)

    def exchange(rows, number):
        def branch(shift):
            pairs = [(a, a ^ shift) for a in range(chan_count)]
            return lambda x: lax.ppermute(x, "chan", pairs)

        branches = [branch(shift) for shift in range(1, chan_count)]
        return lax.switch(number - 1, branches, rows)

    first_other = exchange(local, partner[0, 0])
    second_other = exchange(local, partner[1, 0])
    factor = 1.0 / (W * math.sqrt(local.shape[3]))
    columns = []
    for other_rows in (first_other, second_other):
        columns.append(other_rows)
        columns.append(jnp.stack([-other_rows[1], other_rows[0]]))
    mixed = jnp.stack(columns)
    own = jnp.broadcast_to(local[None], mixed.shape)
    product = jnp.einsum("qpfiw,qpfjw->qfij", own, mixed, preferred_element_type=jnp.float32)
    return (product * factor).reshape(2, 2, bins, width, width)


def solution(mesh):
    return jax.shard_map(
        body,
        mesh=mesh,
        in_specs=(P(("chan", "band"), None, None), P(("chan", "band")), P(), P()),
        out_specs=P(None, None, "band", "chan", None),
        check_vma=False,
    )
```

```python
import math

import jax
import numpy as np
import jax.numpy as jnp
from jax import lax
from jax.sharding import PartitionSpec as P

DEC = 10
TAPS = 63
W = 256
NF = 128
HALF = 32


def mean_matrix(length, half):
    rows = jnp.arange(length, dtype=jnp.int32)[:, None]
    cols = jnp.arange(length, dtype=jnp.int32)[None, :]
    begins = jnp.clip(cols - half, 0, length - 2 * half - 1)
    inside = (rows >= begins) & (rows <= begins + 2 * half)
    return inside.astype(jnp.float32)


def dft_table(length, bins):
    samples = jnp.arange(length, dtype=jnp.int32)[:, None]
    freqs = jnp.arange(bins, dtype=jnp.int32)[None, :]
    phase = samples * freqs % length
    angle = phase.astype(jnp.float32) * (2.0 * math.pi / length)
    return jnp.concatenate([jnp.cos(angle), -jnp.sin(angle)], axis=1)


def filter_table(taps, phases):
    padded = jnp.pad(taps, (0, phases * DEC - TAPS))
    grid = padded.reshape(phases, DEC)
    rows = jnp.arange(W + phases - 1, dtype=jnp.int32)[:, None]
    cols = jnp.arange(W, dtype=jnp.int32)[None, :]
    onehot = (
        (rows - cols)[None, :, :] == jnp.arange(phases, dtype=jnp.int32)[:, None, None]
    ).astype(jnp.bfloat16)
    table = jnp.einsum("jqn,jr->qrn", onehot, grid, preferred_element_type=jnp.float32)
    return table.reshape((W + phases - 1) * DEC, W).astype(jnp.bfloat16)


def window_spectrum(segment, offset, table, level_matrix, transform, blocks, bands):
    span = table.shape[0]
    piece = lax.dynamic_slice_in_dim(segment, offset, span, 1)
    decimated = jnp.dot(piece, table, preferred_element_type=jnp.float32)
    size = jnp.abs(decimated)
    high = size.astype(jnp.bfloat16)
    low = (size - high.astype(jnp.float32)).astype(jnp.bfloat16)
    ones = level_matrix.astype(jnp.bfloat16)
    level = (
        jnp.dot(high, ones, preferred_element_type=jnp.float32)
        + jnp.dot(low, ones, preferred_element_type=jnp.float32)
    ) / (2 * HALF + 1)
    normed = decimated / (level + 1e-05)
    channels = segment.shape[0]
    ordered = np.ascontiguousarray(
        transform.reshape(W, 2, bands, NF // bands).transpose(2, 1, 3, 0).reshape(2 * NF, W)
    )
    spectrum = jnp.einsum(
        "akn,ain->aki",
        jnp.broadcast_to(ordered[None], (blocks, 2 * NF, W)),
        normed.reshape(blocks, channels // blocks, W),
        precision=lax.Precision.HIGH,
    )
    return spectrum.reshape(blocks, bands, 2, NF // bands, channels // blocks).astype(jnp.bfloat16)


def body(raw, offsets, taps, partner):
    phases = (TAPS + DEC - 1) // DEC
    table = filter_table(taps, phases)
    rows_np = np.arange(W)[:, None]
    begins_np = np.clip(np.arange(W)[None, :] - HALF, 0, W - 2 * HALF - 1)
    level_matrix = ((rows_np >= begins_np) & (rows_np <= begins_np + 2 * HALF)).astype(np.float32)
    phase = (np.arange(W)[:, None] * np.arange(NF)[None, :]) % W
    angle = phase.astype(np.float32) * np.float32(2.0 * math.pi / W)
    transform = np.concatenate([np.cos(angle), -np.sin(angle)], axis=1).astype(np.float32)
    chan_count = lax.axis_size("chan")
    band_count = lax.axis_size("band")
    spectrum = window_spectrum(
        raw[0], offsets[0], table, level_matrix, transform, chan_count, band_count
    )
    _, _, part_count, bins, width = spectrum.shape
    arranged = spectrum.transpose(2, 3, 4, 0, 1).reshape(
        part_count, bins, width, chan_count * band_count
    )
    local = lax.all_to_all(arranged, ("chan", "band"), split_axis=3, concat_axis=3, tiled=True)

    def exchange(rows, number):
        def branch(shift):
            pairs = [(a, a ^ shift) for a in range(chan_count)]
            return lambda x: lax.ppermute(x, "chan", pairs)

        branches = [branch(shift) for shift in range(1, chan_count)]
        return lax.switch(number - 1, branches, rows)

    first_other = exchange(local, partner[0, 0])
    second_other = exchange(local, partner[1, 0])
    factor = 1.0 / (W * math.sqrt(local.shape[3]))
    columns = []
    for other_rows in (first_other, second_other):
        columns.append(other_rows)
        columns.append(jnp.stack([-other_rows[1], other_rows[0]]))
    mixed = jnp.stack(columns)
    own = jnp.broadcast_to(local[None], mixed.shape)
    product = jnp.einsum("qpfiw,qpfjw->qfij", own, mixed, preferred_element_type=jnp.float32)
    return (product * factor).reshape(2, 2, bins, width, width)


def solution(mesh):
    return jax.shard_map(
        body,
        mesh=mesh,
        in_specs=(P(("chan", "band"), None, None), P(("chan", "band")), P(), P()),
        out_specs=P(None, None, "band", "chan", None),
        check_vma=False,
    )
```
